1024 devices in a mesh: comp: 16 (over z, y_lo), tile: 64 (over y_hi, x, core).
Axes of the slice: x: 8, y: 8 (y_hi: 4, y_lo: 2; y = y_hi * 2 + y_lo), z: 8, core: 2. Of those that a mesh axis runs over, the one named last changes fastest.
Arguments:
- atm_state: float32 [72, 128, 8192], P(None, 'comp', 'tile'), may hold values from -6 to 6
- kappa: float32 [128, 8192], P('comp', 'tile'), may hold values from 0.02 to 0.2
- vert_mix: float32 [72, 72], replicated, may hold values from -0.375 to 0.375
- flux_proj: float32 [24, 72], replicated, may hold values from -0.75 to 0.75
- remap_weight: bfloat16 [32768, 4, 64, 64], P(('comp', 'tile')), may hold values from -0.375 to 0.375
- remap_cols: int32 [32768, 4], P(('comp', 'tile')), may hold values from 0 to 1023, as said below
- ocean_state: float32 [80, 2097152], P(None, ('comp', 'tile')), may hold values from -6 to 6
- ocean_mix: float32 [80, 80], replicated, may hold values from -0.3125 to 0.3125
- forcing: float32 [80, 24], replicated, may hold values from -1.25 to 1.25
- wet_mask: int32 [2097152], P(('comp', 'tile')), may hold values 0 or 1
- surface_proj: float32 [8, 80], replicated, may hold values from -0.625 to 0.625
- back_weight: bfloat16 [16384, 4, 64, 64], P(('comp', 'tile')), may hold values from -0.375 to 0.375
- back_cols: int32 [16384, 4], P(('comp', 'tile')), may hold values from 0 to 2047, as said below
- back_proj: float32 [72, 8], replicated, may hold values from -2 to 2
Outputs:
- atm_out: float32 [72, 128, 8192], P(None, 'comp', 'tile')
- ocean_out: float32 [80, 2097152], P(None, ('comp', 'tile'))
The draws below stay inside these ranges and needn't reach their ends.
Inputs may be any that keep to these rules, and one draw needn't show every extreme that they name: Indices count the atmosphere blocks of the ocean block's own comp group; the tile of each index, remap_cols // 16, lies within 2 tiles, cyclically over 64 tiles, of the ocean block's own tile (r % 2048) // 32. Indices count the ocean blocks of the atmosphere block's own comp group; the tile of each index, back_cols // 32, lies within 2 tiles, cyclically over 64 tiles, of the atmosphere block's own tile (a % 1024) // 16.
All inputs are finite; a program needn't handle non-finite values. No bound on the sum of `wet_mask` on one device may be relied on, other than what follows from the above.
Results may differ from the reference program's by a relative error of at most 0.0029.
Values may be sent and summed in bfloat16 or wider, within the bound.
No kernel may reach another device: no remote copies, remote signals or barrier semaphores. Data moves between devices by JAX's collectives and lax.ppermute only.
A program may use at most 32 MiB of HBM per device.

```python
import jax
import jax.numpy as jnp
from jax import lax

LEVA = 72
OLEV = 80
NF = 24
NO = 8
KB = 4
AX = 128
AY = 8
OBLK = 32
ABLK = 16
NAY = 128
NAX = 8192
OCELLS = 2097152
OB_TOTAL = 32768
AB_TOTAL = 16384
N_COMP = 16
N_TILE = 64


def nearby_columns(key, rows_total, rows_tile, cols_tile):
    group_rows = N_TILE * rows_tile
    position = jnp.arange(rows_total, dtype=jnp.int32) % group_rows
    own_tile = position // rows_tile
    offsets = jax.random.randint(jax.random.fold_in(key, 11), (rows_total, KB), -2, 3)
    within = jax.random.randint(jax.random.fold_in(key, 12), (rows_total, KB), 0, cols_tile)
    tiles = (own_tile[:, None] + offsets) % N_TILE
    cols = tiles * cols_tile + within
    first = jnp.arange(KB, dtype=jnp.int32)[None, :] == 0
    low = (position[:, None] == 0) & first
    high = (position[:, None] == group_rows - 1) & first
    cols = jnp.where(low, 0, cols)
    cols = jnp.where(high, N_TILE * cols_tile - 1, cols)
    return cols.astype(jnp.int32)


def draw_remap_cols(key, part):
    return nearby_columns(key, OB_TOTAL, OBLK, ABLK)


def draw_back_cols(key, part):
    return nearby_columns(key, AB_TOTAL, ABLK, OBLK)


def touch_ends(values, rng, least, largest):
    dims = values.shape
    spot = [jax.random.randint(jax.random.fold_in(rng, axis), (), 0, dims[axis]) for axis in range(len(dims))]
    values = values.at[tuple(spot)].set(least)
    longest = dims.index(max(dims))
    spot[longest] = (spot[longest] + 1) % dims[longest]
    return values.at[tuple(spot)].set(largest)


def block_levels(key, shape, pieces, low, largest):
    factor_of = 1.0
    for axis_at, blocks in pieces:
        steps = jax.random.uniform(jax.random.fold_in(jax.random.fold_in(key, 6), axis_at), (blocks,), jnp.float32, low / len(pieces), largest / len(pieces))
        factor_of = factor_of * jnp.repeat(jnp.exp(steps), shape[axis_at] // blocks).reshape((-1,) + (1,) * (len(shape) - 1 - axis_at))
    return factor_of


def normal_values(key, extent, spread, limit, pieces=(), kind=jnp.bfloat16):
    values = spread * jax.random.normal(key, extent, jnp.float32)
    if pieces:
        values = values * block_levels(key, extent, pieces, -0.22, 0.18)
    return jnp.clip(values, -limit, limit).astype(kind)


def setup_inputs(seed: int = 0) -> dict:
    key_of = jax.random.split(jax.random.key(seed), 15)
    atm_state = normal_values(key_of[0], (LEVA, NAY, NAX), 1.0, 6.0, ((1, 16), (2, 64)), jnp.float32)
    kappa = jnp.clip(0.02 + 0.18 * jax.random.uniform(key_of[1], (NAY, NAX), jnp.float32) ** block_levels(key_of[1], (NAY, NAX), ((0, 16), (1, 64)), -0.2, 0.2), 0.02, 0.2)
    vert_mix = normal_values(key_of[2], (LEVA, LEVA), (4 * LEVA) ** -0.5, 0.375, (), jnp.float32)
    flux_proj = normal_values(key_of[3], (NF, LEVA), LEVA ** -0.5, 0.75, (), jnp.float32)
    remap_weight = normal_values(key_of[4], (OB_TOTAL, KB, 64, 64), (64 * KB) ** -0.5, 0.375, ((0, 1024),))
    remap_cols = draw_remap_cols(jax.random.fold_in(key_of[14], 71), 0)
    ocean_state = normal_values(key_of[6], (OLEV, OCELLS), 1.0, 6.0, ((1, 1024),), jnp.float32)
    ocean_mix = normal_values(key_of[7], (OLEV, OLEV), (4 * OLEV) ** -0.5, 0.3125, (), jnp.float32)
    forcing = normal_values(key_of[8], (OLEV, NF), NF ** -0.5, 1.25, (), jnp.float32)
    wet_mask = touch_ends((jax.random.randint(key_of[9], (OCELLS,), 0, 10) < 7).astype(jnp.int32), jax.random.fold_in(key_of[9], 1), 0, 1)
    surface_proj = normal_values(key_of[10], (NO, OLEV), OLEV ** -0.5, 0.625, (), jnp.float32)
    back_weight = normal_values(key_of[11], (AB_TOTAL, KB, 64, 64), (64 * KB) ** -0.5, 0.375, ((0, 1024),))
    back_cols = draw_back_cols(jax.random.fold_in(key_of[14], 71), 0)
    back_proj = normal_values(key_of[13], (LEVA, NO), NO ** -0.5, 2.0, (), jnp.float32)
    return dict(atm_state=atm_state, kappa=kappa, vert_mix=vert_mix, flux_proj=flux_proj, remap_weight=remap_weight, remap_cols=remap_cols, ocean_state=ocean_state, ocean_mix=ocean_mix, forcing=forcing, wet_mask=wet_mask, surface_proj=surface_proj, back_weight=back_weight, back_cols=back_cols, back_proj=back_proj)


def level_mix(matrix, field):
    flat = field.reshape(field.shape[0], -1)
    return jnp.dot(matrix, flat, precision=lax.Precision.HIGHEST).reshape((matrix.shape[0],) + field.shape[1:])


def substep(field, kappa, vert_mix):
    beside_all = jnp.roll(field, 1, 1) + jnp.roll(field, -1, 1) + jnp.roll(field, 1, 2) + jnp.roll(field, -1, 2)
    return field + kappa[None] * (beside_all - 4.0 * field) + level_mix(vert_mix, field)


def remap_group(blocks, cols, weights):
    picked = blocks[:, cols].astype(jnp.float32)
    return jnp.einsum('okij,fokj->foi', weights.astype(jnp.float32), picked, precision=lax.Precision.HIGHEST)


def reference(atm_state, kappa, vert_mix, flux_proj, remap_weight, remap_cols, ocean_state, ocean_mix, forcing, wet_mask, surface_proj, back_weight, back_cols, back_proj):
    atm_mid = substep(substep(atm_state, kappa, vert_mix), kappa, vert_mix)
    surface = level_mix(flux_proj, atm_mid).astype(jnp.bfloat16)
    grouped = surface.reshape(NF, N_COMP, AY, N_TILE, AX).transpose(1, 0, 3, 2, 4).reshape(N_COMP, NF, N_TILE * ABLK, 64)
    cols = remap_cols.reshape(N_COMP, N_TILE * OBLK, KB)
    weights = remap_weight.reshape(N_COMP, N_TILE * OBLK, KB, 64, 64)
    remapped = lax.map(lambda item: remap_group(item[0], item[1], item[2]), (grouped, cols, weights))
    remapped = remapped.transpose(1, 0, 2, 3).reshape(NF, OCELLS)
    stepped = ocean_state + jnp.dot(ocean_mix, ocean_state, precision=lax.Precision.HIGHEST) + jnp.dot(forcing, remapped, precision=lax.Precision.HIGHEST)
    ocean_out = jnp.where(wet_mask[None] == 1, stepped, ocean_state)
    sea = jnp.dot(surface_proj, ocean_out, precision=lax.Precision.HIGHEST).astype(jnp.bfloat16)
    sea_grouped = sea.reshape(NO, N_COMP, N_TILE * OBLK, 64).transpose(1, 0, 2, 3)
    bcols = back_cols.reshape(N_COMP, N_TILE * ABLK, KB)
    bweights = back_weight.reshape(N_COMP, N_TILE * ABLK, KB, 64, 64)
    returned = lax.map(lambda item: remap_group(item[0], item[1], item[2]), (sea_grouped, bcols, bweights))
    returned = returned.reshape(N_COMP, NO, N_TILE, AY, AX).transpose(1, 0, 3, 2, 4).reshape(NO, NAY, NAX)
    atm_out = atm_mid + level_mix(back_proj, returned)
    return atm_out, ocean_out
```

```python
import jax
import jax.numpy as jnp
from jax import lax
from jax.sharding import PartitionSpec as P


def from_behind(value, axis, steps):
    count = lax.axis_size(axis)
    pairs = [(source, (source + steps) % count) for source in range(count)]
    return lax.ppermute(value, axis, pairs)


def halo_cols(cells, width):
    levels, rows, cols = cells.shape
    head = cells[:, :, :width].reshape(-1)
    tail = cells[:, :, cols - width:].reshape(-1)
    left = from_behind(tail, "tile", 1).reshape(levels, rows, width)
    right = from_behind(head, "tile", -1).reshape(levels, rows, width)
    return jnp.concatenate([left, cells, right], axis=2)


def halo_rows(cells, width):
    levels, rows, cols = cells.shape
    head = cells[:, :width, :]
    tail = cells[:, rows - width:, :]
    up = from_behind(tail, "comp", 1)
    down = from_behind(head, "comp", -1)
    return jnp.concatenate([up, cells, down], axis=1)


def level_mix(matrix, field):
    return jnp.einsum("ml,l...->m...", matrix, field, precision=lax.Precision.HIGHEST)


def inner_step(padded, coeff, vert_mix):
    center = padded[:, 1:-1, 1:-1]
    beside_all = (
        padded[:, 2:, 1:-1] + padded[:, :-2, 1:-1] + padded[:, 1:-1, 2:] + padded[:, 1:-1, :-2]
    )
    return center + coeff[None] * (beside_all - 4.0 * center) + level_mix(vert_mix, center)


def block_product(weights, picked):
    return jnp.einsum("okij,fokj->foi", weights, picked, preferred_element_type=jnp.float32)


def near_index(cols, per_tile, tiles, here):
    relative = (cols // per_tile - here + 2) % tiles
    return relative * per_tile + cols % per_tile


def body(
    atm_state,
    kappa,
    vert_mix,
    flux_proj,
    remap_weight,
    remap_cols,
    ocean_state,
    ocean_mix,
    forcing,
    wet_mask,
    surface_proj,
    back_weight,
    back_cols,
    back_proj,
):
    levels, rows_here, cols_here = atm_state.shape
    joined = jnp.concatenate([atm_state, kappa[None]], axis=0)
    padded = halo_rows(halo_cols(joined, 2), 2)
    field = padded[:levels]
    coeff = padded[levels]
    first = inner_step(field, coeff[1:-1, 1:-1], vert_mix)
    atm_mid = inner_step(first, coeff[2:-2, 2:-2], vert_mix)
    surface = level_mix(flux_proj, atm_mid).astype(jnp.bfloat16)
    fields = surface.shape[0]
    atm_blocks = rows_here * cols_here // 64
    surface_blocks = surface.reshape(fields, atm_blocks, 64)
    ocean_blocks = remap_weight.shape[0]
    tiles = lax.axis_size("tile")
    here = lax.axis_index("tile")
    pieces = []
    for offset in (-2, -1, 0, 1, 2):
        if offset == 0:
            pieces.append(surface_blocks)
        else:
            pieces.append(from_behind(surface_blocks, "tile", -offset))
    nearby = jnp.concatenate(pieces, 1)
    local = near_index(remap_cols, atm_blocks, tiles, here)
    remapped = block_product(remap_weight, nearby[:, local])
    remapped = remapped.reshape(fields, ocean_blocks * 64)
    stepped = (
        ocean_state
        + jnp.dot(ocean_mix, ocean_state, precision=lax.Precision.HIGHEST)
        + jnp.dot(forcing, remapped, precision=lax.Precision.HIGHEST)
    )
    ocean_out = jnp.where(wet_mask[None] == 1, stepped, ocean_state)
    sea = jnp.dot(surface_proj, ocean_out, precision=lax.Precision.HIGHEST).astype(jnp.bfloat16)
    sea_blocks = sea.reshape(sea.shape[0], ocean_blocks, 64)
    sea_pieces = []
    for offset in (-2, -1, 0, 1, 2):
        if offset == 0:
            sea_pieces.append(sea_blocks)
        else:
            sea_pieces.append(from_behind(sea_blocks, "tile", -offset))
    sea_nearby = jnp.concatenate(sea_pieces, 1)
    back_local = near_index(back_cols, ocean_blocks, tiles, here)
    returned = block_product(back_weight, sea_nearby[:, back_local])
    returned = returned.reshape(sea.shape[0], rows_here, cols_here)
    atm_out = atm_mid + level_mix(back_proj, returned)
    return (atm_out, ocean_out)


def solution(mesh):
    return jax.shard_map(
        body,
        mesh=mesh,
        in_specs=(
            P(None, "comp", "tile"),
            P("comp", "tile"),
            P(),
            P(),
            P(("comp", "tile"), None, None, None),
            P(("comp", "tile"), None),
            P(None, ("comp", "tile")),
            P(),
            P(),
            P(("comp", "tile")),
            P(),
            P(("comp", "tile"), None, None, None),
            P(("comp", "tile"), None),
            P(),
        ),
        out_specs=(P(None, "comp", "tile"), P(None, ("comp", "tile"))),
        check_vma=False,
    )
```

```python
import jax
import jax.numpy as jnp
from jax import lax
from jax.sharding import PartitionSpec as P


def from_behind(value, axis, steps):
    count = lax.axis_size(axis)
    pairs = [(source, (source + steps) % count) for source in range(count)]
    return lax.ppermute(value, axis, pairs)


def halo_cols(cells, width):
    levels, rows, cols = cells.shape
    head = cells[:, :, :width].reshape(-1)
    tail = cells[:, :, cols - width:].reshape(-1)
    left = from_behind(tail, "tile", 1).reshape(levels, rows, width)
    right = from_behind(head, "tile", -1).reshape(levels, rows, width)
    return jnp.concatenate([left, cells, right], axis=2)


def halo_rows(cells, width):
    levels, rows, cols = cells.shape
    head = cells[:, :width, :]
    tail = cells[:, rows - width:, :]
    up = from_behind(tail, "comp", 1)
    down = from_behind(head, "comp", -1)
    return jnp.concatenate([up, cells, down], axis=1)


def level_mix(matrix, field):
    return jnp.einsum("ml,l...->m...", matrix, field, precision=lax.Precision.HIGHEST)


def inner_step(padded, coeff, vert_mix):
    center = padded[:, 1:-1, 1:-1]
    beside_all = (
        padded[:, 2:, 1:-1] + padded[:, :-2, 1:-1] + padded[:, 1:-1, 2:] + padded[:, 1:-1, :-2]
    )
    return center + coeff[None] * (beside_all - 4.0 * center) + level_mix(vert_mix, center)


def block_product(weights, picked):
    return jnp.einsum("okij,fokj->foi", weights, picked, preferred_element_type=jnp.float32)


def near_index(cols, per_tile, tiles, here):
    relative = (cols // per_tile - here + 2) % tiles
    return relative * per_tile + cols % per_tile


def exchange_and_pick(blocks, cols, here):
    fields, per_tile, cells = blocks.shape
    tiles = lax.axis_size("tile")
    local = near_index(cols, per_tile, tiles, here).reshape(-1)
    picked = None
    for slot, offset in enumerate((-2, -1, 0, 1, 2)):
        piece = blocks if offset == 0 else from_behind(blocks, "tile", -offset)
        ids = slot * per_tile + jnp.arange(per_tile, dtype=local.dtype)
        onehot = (local[:, None] == ids[None, :]).astype(blocks.dtype)
        part = jnp.einsum("qb,fbj->fqj", onehot, piece, preferred_element_type=jnp.float32)
        picked = part if picked is None else picked + part
    return picked.astype(blocks.dtype).reshape((fields,) + cols.shape + (cells,))


def body(
    atm_state,
    kappa,
    vert_mix,
    flux_proj,
    remap_weight,
    remap_cols,
    ocean_state,
    ocean_mix,
    forcing,
    wet_mask,
    surface_proj,
    back_weight,
    back_cols,
    back_proj,
):
    levels, rows_here, cols_here = atm_state.shape
    joined = jnp.concatenate([atm_state, kappa[None]], axis=0)
    padded = halo_rows(halo_cols(joined, 2), 2)
    field = padded[:levels]
    coeff = padded[levels]
    first = inner_step(field, coeff[1:-1, 1:-1], vert_mix)
    atm_mid = inner_step(first, coeff[2:-2, 2:-2], vert_mix)
    surface = level_mix(flux_proj, atm_mid).astype(jnp.bfloat16)
    fields = surface.shape[0]
    atm_blocks = rows_here * cols_here // 64
    surface_blocks = surface.reshape(fields, atm_blocks, 64)
    ocean_blocks = remap_weight.shape[0]
    here = lax.axis_index("tile")
    mixed = lax.optimization_barrier(
        ocean_state + jnp.dot(ocean_mix, ocean_state, precision=lax.Precision.HIGHEST)
    )
    remapped = block_product(remap_weight, exchange_and_pick(surface_blocks, remap_cols, here))
    remapped = remapped.reshape(fields, ocean_blocks * 64)
    stepped = mixed + jnp.dot(forcing, remapped, precision=lax.Precision.HIGHEST)
    ocean_out = jnp.where(wet_mask[None] == 1, stepped, ocean_state)
    sea = jnp.dot(surface_proj, ocean_out, precision=lax.Precision.HIGHEST).astype(jnp.bfloat16)
    sea_blocks = sea.reshape(sea.shape[0], ocean_blocks, 64)
    returned = block_product(back_weight, exchange_and_pick(sea_blocks, back_cols, here))
    returned = returned.reshape(sea.shape[0], rows_here, cols_here)
    atm_out = atm_mid + level_mix(back_proj, returned)
    return (atm_out, ocean_out)


def solution(mesh):
    return jax.shard_map(
        body,
        mesh=mesh,
        in_specs=(
            P(None, "comp", "tile"),
            P("comp", "tile"),
            P(),
            P(),
            P(("comp", "tile"), None, None, None),
            P(("comp", "tile"), None),
            P(None, ("comp", "tile")),
            P(),
            P(),
            P(("comp", "tile")),
            P(),
            P(("comp", "tile"), None, None, None),
            P(("comp", "tile"), None),
            P(),
        ),
        out_specs=(P(None, "comp", "tile"), P(None, ("comp", "tile"))),
        check_vma=False,
    )
```

```python
import jax
import jax.numpy as jnp
from jax import lax
from jax.sharding import PartitionSpec as P


def from_behind(value, axis, steps):
    count = lax.axis_size(axis)
    pairs = [(source, (source + steps) % count) for source in range(count)]
    return lax.ppermute(value, axis, pairs)


def halo_cols(cells, width):
    levels, rows, cols = cells.shape
    head = cells[:, :, :width].reshape(-1)
    tail = cells[:, :, cols - width:].reshape(-1)
    left = from_behind(tail, "tile", 1).reshape(levels, rows, width)
    right = from_behind(head, "tile", -1).reshape(levels, rows, width)
    return jnp.concatenate([left, cells, right], axis=2)


def halo_rows(cells, width):
    levels, rows, cols = cells.shape
    head = cells[:, :width, :]
    tail = cells[:, rows - width:, :]
    up = from_behind(tail, "comp", 1)
    down = from_behind(head, "comp", -1)
    return jnp.concatenate([up, cells, down], axis=1)


def level_mix(matrix, field):
    return jnp.einsum("ml,l...->m...", matrix, field, precision=lax.Precision.HIGHEST)


def inner_step(padded, coeff, vert_mix):
    center = padded[:, 1:-1, 1:-1]
    beside_all = (
        padded[:, 2:, 1:-1] + padded[:, :-2, 1:-1] + padded[:, 1:-1, 2:] + padded[:, 1:-1, :-2]
    )
    return center + coeff[None] * (beside_all - 4.0 * center) + level_mix(vert_mix, center)


def block_product(weights, picked):
    return jnp.einsum("okij,fokj->foi", weights, picked, preferred_element_type=jnp.float32)


def near_index(cols, per_tile, tiles, here):
    relative = (cols // per_tile - here + 2) % tiles
    return relative * per_tile + cols % per_tile


def pick(local, base, piece, count):
    ids = base + jnp.arange(count, dtype=local.dtype)
    onehot = (local[:, None] == ids[None, :]).astype(piece.dtype)
    return jnp.einsum("qb,fbj->fqj", onehot, piece, preferred_element_type=jnp.float32)


def exchange_and_pick(blocks, cols, here):
    fields, per_tile, cells = blocks.shape
    tiles = lax.axis_size("tile")
    local = near_index(cols, per_tile, tiles, here).reshape(-1)
    behind = from_behind(blocks, "tile", 2)
    ahead = from_behind(blocks, "tile", -2)
    even = here % 2 == 0
    forward = jnp.where(even, ahead, behind)
    bundle = jnp.concatenate([blocks, forward], axis=1)
    partner = lax.ppermute(bundle, "tile", [(s, s ^ 1) for s in range(tiles)])
    plus_one = jnp.where(even, 0, per_tile)
    minus_one = per_tile - plus_one
    ids = jnp.arange(per_tile, dtype=local.dtype)
    slot = local // per_tile
    within = local % per_tile
    partner_local = jnp.where(slot == 3, plus_one + within, jnp.where(slot == 1, minus_one + within, -1))
    picked = pick(local, 2 * per_tile, blocks, per_tile)
    picked = picked + pick(local, 0, behind, per_tile)
    picked = picked + pick(local, 4 * per_tile, ahead, per_tile)
    picked = picked + pick(partner_local, 0, partner, 2 * per_tile)
    return picked.astype(blocks.dtype).reshape((fields,) + cols.shape + (cells,))


def body(
    atm_state,
    kappa,
    vert_mix,
    flux_proj,
    remap_weight,
    remap_cols,
    ocean_state,
    ocean_mix,
    forcing,
    wet_mask,
    surface_proj,
    back_weight,
    back_cols,
    back_proj,
):
    levels, rows_here, cols_here = atm_state.shape
    joined = jnp.concatenate([atm_state, kappa[None]], axis=0)
    padded = halo_rows(halo_cols(joined, 2), 2)
    field = padded[:levels]
    coeff = padded[levels]
    first = inner_step(field, coeff[1:-1, 1:-1], vert_mix)
    atm_mid = inner_step(first, coeff[2:-2, 2:-2], vert_mix)
    surface = level_mix(flux_proj, atm_mid).astype(jnp.bfloat16)
    fields = surface.shape[0]
    atm_blocks = rows_here * cols_here // 64
    surface_blocks = surface.reshape(fields, atm_blocks, 64)
    ocean_blocks = remap_weight.shape[0]
    here = lax.axis_index("tile")
    mixed = lax.optimization_barrier(
        ocean_state + jnp.dot(ocean_mix, ocean_state, precision=lax.Precision.HIGHEST)
    )
    remapped = block_product(remap_weight, exchange_and_pick(surface_blocks, remap_cols, here))
    remapped = remapped.reshape(fields, ocean_blocks * 64)
    stepped = mixed + jnp.dot(forcing, remapped, precision=lax.Precision.HIGHEST)
    ocean_out = jnp.where(wet_mask[None] == 1, stepped, ocean_state)
    sea = jnp.dot(surface_proj, ocean_out, precision=lax.Precision.HIGHEST).astype(jnp.bfloat16)
    sea_blocks = sea.reshape(sea.shape[0], ocean_blocks, 64)
    returned = block_product(back_weight, exchange_and_pick(sea_blocks, back_cols, here))
    returned = returned.reshape(sea.shape[0], rows_here, cols_here)
    atm_out = atm_mid + level_mix(back_proj, returned)
    return (atm_out, ocean_out)


def solution(mesh):
    return jax.shard_map(
        body,
        mesh=mesh,
        in_specs=(
            P(None, "comp", "tile"),
            P("comp", "tile"),
            P(),
            P(),
            P(("comp", "tile"), None, None, None),
            P(("comp", "tile"), None),
            P(None, ("comp", "tile")),
            P(),
            P(),
            P(("comp", "tile")),
            P(),
            P(("comp", "tile"), None, None, None),
            P(("comp", "tile"), None),
            P(),
        ),
        out_specs=(P(None, "comp", "tile"), P(None, ("comp", "tile"))),
        check_vma=False,
    )
```

```python
import jax
import jax.numpy as jnp
from jax import lax
from jax.sharding import PartitionSpec as P


def from_behind(value, axis, steps):
    count = lax.axis_size(axis)
    pairs = [(source, (source + steps) % count) for source in range(count)]
    return lax.ppermute(value, axis, pairs)


def swap(value, axis, stride, phase):
    count = lax.axis_size(axis)
    groups = count // stride
    pairs = []
    for source in range(count):
        group = source // stride
        step = 1 if group % 2 == phase else -1
        pairs.append((source, ((group + step) % groups) * stride + source % stride))
    return lax.ppermute(value, axis, pairs)


def halo_cols(cells, width):
    levels, rows, cols = cells.shape
    even = lax.axis_index("tile") % 2 == 0
    head = cells[:, :, :width].reshape(-1)
    tail = cells[:, :, cols - width:].reshape(-1)
    partner = swap(jnp.where(even, tail, head), "tile", 1, 0)
    cross = swap(jnp.where(even, head, tail), "tile", 1, 1)
    left = jnp.where(even, cross, partner).reshape(levels, rows, width)
    right = jnp.where(even, partner, cross).reshape(levels, rows, width)
    return jnp.concatenate([left, cells, right], axis=2)


def halo_rows(cells, width):
    levels, rows, cols = cells.shape
    even = lax.axis_index("comp") % 2 == 0
    head = cells[:, :width, :]
    tail = cells[:, rows - width:, :]
    first = swap(jnp.where(even, tail, head), "comp", 1, 0)
    second = swap(jnp.where(even, head, tail), "comp", 1, 1)
    up = jnp.where(even, second, first)
    down = jnp.where(even, first, second)
    return jnp.concatenate([up, cells, down], axis=1)


def level_mix(matrix, field):
    return jnp.einsum("ml,l...->m...", matrix, field, precision=lax.Precision.HIGHEST)


def inner_step(padded, coeff, vert_mix):
    center = padded[:, 1:-1, 1:-1]
    beside_all = (
        padded[:, 2:, 1:-1] + padded[:, :-2, 1:-1] + padded[:, 1:-1, 2:] + padded[:, 1:-1, :-2]
    )
    return center + coeff[None] * (beside_all - 4.0 * center) + level_mix(vert_mix, center)


def block_product(weights, picked):
    return jnp.einsum("okij,fokj->foi", weights, picked, preferred_element_type=jnp.float32)


def near_index(cols, per_tile, tiles, here):
    relative = (cols // per_tile - here + 2) % tiles
    return relative * per_tile + cols % per_tile


def pick(local, base, piece, count):
    ids = base + jnp.arange(count, dtype=local.dtype)
    onehot = (local[:, None] == ids[None, :]).astype(piece.dtype)
    return jnp.einsum("qb,fbj->fqj", onehot, piece, preferred_element_type=jnp.float32)


def exchange_and_pick(blocks, cols, here):
    fields, per_tile, cells = blocks.shape
    tiles = lax.axis_size("tile")
    local = near_index(cols, per_tile, tiles, here).reshape(-1)
    even = here % 2 == 0
    chip_even = (here // 2) % 2 == 0
    first = swap(blocks, "tile", 2, 0)
    second = swap(blocks, "tile", 2, 1)
    first_base = jnp.where(chip_even, 4 * per_tile, 0)
    second_base = 4 * per_tile - first_base
    forward = jnp.where(even == chip_even, first, second)
    bundle = jnp.concatenate([blocks, forward], axis=1)
    partner = swap(bundle, "tile", 1, 0)
    plus_one = jnp.where(even, 0, per_tile)
    minus_one = per_tile - plus_one
    slot = local // per_tile
    within = local % per_tile
    partner_local = jnp.where(slot == 3, plus_one + within, jnp.where(slot == 1, minus_one + within, -1))
    picked = pick(local, 2 * per_tile, blocks, per_tile)
    picked = picked + pick(local, first_base, first, per_tile)
    picked = picked + pick(local, second_base, second, per_tile)
    picked = picked + pick(partner_local, 0, partner, 2 * per_tile)
    return picked.astype(blocks.dtype).reshape((fields,) + cols.shape + (cells,))


def body(
    atm_state,
    kappa,
    vert_mix,
    flux_proj,
    remap_weight,
    remap_cols,
    ocean_state,
    ocean_mix,
    forcing,
    wet_mask,
    surface_proj,
    back_weight,
    back_cols,
    back_proj,
):
    levels, rows_here, cols_here = atm_state.shape
    joined = jnp.concatenate([atm_state, kappa[None]], axis=0)
    padded = halo_rows(halo_cols(joined, 2), 2)
    field = padded[:levels]
    coeff = padded[levels]
    first = inner_step(field, coeff[1:-1, 1:-1], vert_mix)
    atm_mid = inner_step(first, coeff[2:-2, 2:-2], vert_mix)
    surface = level_mix(flux_proj, atm_mid).astype(jnp.bfloat16)
    fields = surface.shape[0]
    atm_blocks = rows_here * cols_here // 64
    surface_blocks = surface.reshape(fields, atm_blocks, 64)
    ocean_blocks = remap_weight.shape[0]
    here = lax.axis_index("tile")
    mixed = lax.optimization_barrier(
        ocean_state + jnp.dot(ocean_mix, ocean_state, precision=lax.Precision.HIGHEST)
    )
    remapped = block_product(remap_weight, exchange_and_pick(surface_blocks, remap_cols, here))
    remapped = remapped.reshape(fields, ocean_blocks * 64)
    stepped = mixed + jnp.dot(forcing, remapped, precision=lax.Precision.HIGHEST)
    ocean_out = jnp.where(wet_mask[None] == 1, stepped, ocean_state)
    sea = jnp.dot(surface_proj, ocean_out, precision=lax.Precision.HIGHEST).astype(jnp.bfloat16)
    sea_blocks = sea.reshape(sea.shape[0], ocean_blocks, 64)
    returned = block_product(back_weight, exchange_and_pick(sea_blocks, back_cols, here))
    returned = returned.reshape(sea.shape[0], rows_here, cols_here)
    atm_out = atm_mid + level_mix(back_proj, returned)
    return (atm_out, ocean_out)


def solution(mesh):
    return jax.shard_map(
        body,
        mesh=mesh,
        in_specs=(
            P(None, "comp", "tile"),
            P("comp", "tile"),
            P(),
            P(),
            P(("comp", "tile"), None, None, None),
            P(("comp", "tile"), None),
            P(None, ("comp", "tile")),
            P(),
            P(),
            P(("comp", "tile")),
            P(),
            P(("comp", "tile"), None, None, None),
            P(("comp", "tile"), None),
            P(),
        ),
        out_specs=(P(None, "comp", "tile"), P(None, ("comp", "tile"))),
        check_vma=False,
    )
```

```python
import jax
import jax.numpy as jnp
from jax import lax
from jax.sharding import PartitionSpec as P


def from_behind(value, axis, steps):
    count = lax.axis_size(axis)
    pairs = [(source, (source + steps) % count) for source in range(count)]
    return lax.ppermute(value, axis, pairs)


def swap(value, axis, stride, phase):
    count = lax.axis_size(axis)
    groups = count // stride
    pairs = []
    for source in range(count):
        group = source // stride
        step = 1 if group % 2 == phase else -1
        pairs.append((source, ((group + step) % groups) * stride + source % stride))
    return lax.ppermute(value, axis, pairs)


def halo_cols(field, coeff, width):
    levels, rows, cols = field.shape
    even = lax.axis_index("tile") % 2 == 0
    cut = levels * rows * width

    def strip(start):
        return jnp.concatenate(
            [field[:, :, start:start + width].reshape(-1), coeff[:, start:start + width].reshape(-1)]
        )

    head = strip(0)
    tail = strip(cols - width)
    partner = swap(jnp.where(even, tail, head), "tile", 1, 0)
    cross = swap(jnp.where(even, head, tail), "tile", 1, 1)
    left = jnp.where(even, cross, partner)
    right = jnp.where(even, partner, cross)
    field = jnp.concatenate(
        [left[:cut].reshape(levels, rows, width), field, right[:cut].reshape(levels, rows, width)],
        axis=2,
    )
    coeff = jnp.concatenate(
        [left[cut:].reshape(rows, width), coeff, right[cut:].reshape(rows, width)], axis=1
    )
    return field, coeff


def halo_rows(field, coeff, width):
    levels, rows, cols = field.shape
    even = lax.axis_index("comp") % 2 == 0
    cut = levels * width * cols

    def strip(start):
        return jnp.concatenate(
            [field[:, start:start + width, :].reshape(-1), coeff[start:start + width, :].reshape(-1)]
        )

    head = strip(0)
    tail = strip(rows - width)
    first = swap(jnp.where(even, tail, head), "comp", 1, 0)
    second = swap(jnp.where(even, head, tail), "comp", 1, 1)
    up = jnp.where(even, second, first)
    down = jnp.where(even, first, second)
    field = jnp.concatenate(
        [up[:cut].reshape(levels, width, cols), field, down[:cut].reshape(levels, width, cols)],
        axis=1,
    )
    coeff = jnp.concatenate(
        [up[cut:].reshape(width, cols), coeff, down[cut:].reshape(width, cols)], axis=0
    )
    return field, coeff


def level_mix(matrix, field):
    return jnp.einsum("ml,l...->m...", matrix, field, precision=lax.Precision.HIGHEST)


def inner_step(padded, coeff, vert_mix):
    center = padded[:, 1:-1, 1:-1]
    beside_all = (
        padded[:, 2:, 1:-1] + padded[:, :-2, 1:-1] + padded[:, 1:-1, 2:] + padded[:, 1:-1, :-2]
    )
    return center + coeff[None] * (beside_all - 4.0 * center) + level_mix(vert_mix, center)


def block_product(weights, picked):
    return jnp.einsum("okij,fokj->foi", weights, picked, preferred_element_type=jnp.float32)


def near_index(cols, per_tile, tiles, here):
    relative = (cols // per_tile - here + 2) % tiles
    return relative * per_tile + cols % per_tile


def pick(local, base, piece, count):
    ids = base + jnp.arange(count, dtype=local.dtype)
    onehot = (local[:, None] == ids[None, :]).astype(piece.dtype)
    return jnp.einsum("qb,fbj->fqj", onehot, piece, preferred_element_type=jnp.float32)


def exchange_and_pick(blocks, cols, here):
    fields, per_tile, cells = blocks.shape
    tiles = lax.axis_size("tile")
    local = near_index(cols, per_tile, tiles, here).reshape(-1)
    even = here % 2 == 0
    chip_even = (here // 2) % 2 == 0
    first = swap(blocks, "tile", 2, 0)
    second = swap(blocks, "tile", 2, 1)
    first_base = jnp.where(chip_even, 4 * per_tile, 0)
    second_base = 4 * per_tile - first_base
    forward = jnp.where(even == chip_even, first, second)
    bundle = jnp.concatenate([blocks, forward], axis=1)
    partner = swap(bundle, "tile", 1, 0)
    plus_one = jnp.where(even, 0, per_tile)
    minus_one = per_tile - plus_one
    slot = local // per_tile
    within = local % per_tile
    partner_local = jnp.where(slot == 3, plus_one + within, jnp.where(slot == 1, minus_one + within, -1))
    picked = pick(local, 2 * per_tile, blocks, per_tile)
    picked = picked + pick(local, first_base, first, per_tile)
    picked = picked + pick(local, second_base, second, per_tile)
    picked = picked + pick(partner_local, 0, partner, 2 * per_tile)
    return picked.astype(blocks.dtype).reshape((fields,) + cols.shape + (cells,))


def body(
    atm_state,
    kappa,
    vert_mix,
    flux_proj,
    remap_weight,
    remap_cols,
    ocean_state,
    ocean_mix,
    forcing,
    wet_mask,
    surface_proj,
    back_weight,
    back_cols,
    back_proj,
):
    levels, rows_here, cols_here = atm_state.shape
    field, coeff = halo_rows(*halo_cols(atm_state, kappa, 2), 2)
    first = inner_step(field, coeff[1:-1, 1:-1], vert_mix)
    atm_mid = inner_step(first, coeff[2:-2, 2:-2], vert_mix)
    surface = level_mix(flux_proj, atm_mid).astype(jnp.bfloat16)
    fields = surface.shape[0]
    atm_blocks = rows_here * cols_here // 64
    surface_blocks = surface.reshape(fields, atm_blocks, 64)
    ocean_blocks = remap_weight.shape[0]
    here = lax.axis_index("tile")
    mixed = lax.optimization_barrier(
        ocean_state + jnp.dot(ocean_mix, ocean_state, precision=lax.Precision.HIGHEST)
    )
    remapped = block_product(remap_weight, exchange_and_pick(surface_blocks, remap_cols, here))
    remapped = remapped.reshape(fields, ocean_blocks * 64)
    stepped = mixed + jnp.dot(forcing, remapped, precision=lax.Precision.HIGHEST)
    ocean_out = jnp.where(wet_mask[None] == 1, stepped, ocean_state)
    sea = jnp.dot(surface_proj, ocean_out, precision=lax.Precision.HIGHEST).astype(jnp.bfloat16)
    sea_blocks = sea.reshape(sea.shape[0], ocean_blocks, 64)
    returned = block_product(back_weight, exchange_and_pick(sea_blocks, back_cols, here))
    returned = returned.reshape(sea.shape[0], rows_here, cols_here)
    atm_out = atm_mid + level_mix(back_proj, returned)
    return (atm_out, ocean_out)


def solution(mesh):
    return jax.shard_map(
        body,
        mesh=mesh,
        in_specs=(
            P(None, "comp", "tile"),
            P("comp", "tile"),
            P(),
            P(),
            P(("comp", "tile"), None, None, None),
            P(("comp", "tile"), None),
            P(None, ("comp", "tile")),
            P(),
            P(),
            P(("comp", "tile")),
            P(),
            P(("comp", "tile"), None, None, None),
            P(("comp", "tile"), None),
            P(),
        ),
        out_specs=(P(None, "comp", "tile"), P(None, ("comp", "tile"))),
        check_vma=False,
    )
```

```python
import jax
import jax.numpy as jnp
from jax import lax
from jax.sharding import PartitionSpec as P


def from_behind(value, axis, steps):
    count = lax.axis_size(axis)
    pairs = [(source, (source + steps) % count) for source in range(count)]
    return lax.ppermute(value, axis, pairs)


def swap(value, axis, stride, phase):
    count = lax.axis_size(axis)
    groups = count // stride
    pairs = []
    for source in range(count):
        group = source // stride
        step = 1 if group % 2 == phase else -1
        pairs.append((source, ((group + step) % groups) * stride + source % stride))
    return lax.ppermute(value, axis, pairs)


def halo_cols(cells, width):
    levels, rows, cols = cells.shape
    even = lax.axis_index("tile") % 2 == 0
    head = cells[:, :, :width].reshape(-1)
    tail = cells[:, :, cols - width:].reshape(-1)
    partner = swap(jnp.where(even, tail, head), "tile", 1, 0)
    cross = swap(jnp.where(even, head, tail), "tile", 1, 1)
    left = jnp.where(even, cross, partner).reshape(levels, rows, width)
    right = jnp.where(even, partner, cross).reshape(levels, rows, width)
    return jnp.concatenate([left, cells, right], axis=2)


def halo_rows(cells, width):
    levels, rows, cols = cells.shape
    even = lax.axis_index("comp") % 2 == 0
    head = cells[:, :width, :]
    tail = cells[:, rows - width:, :]
    first = swap(jnp.where(even, tail, head), "comp", 1, 0)
    second = swap(jnp.where(even, head, tail), "comp", 1, 1)
    up = jnp.where(even, second, first)
    down = jnp.where(even, first, second)
    return jnp.concatenate([up, cells, down], axis=1)


def level_mix(matrix, field):
    return jnp.einsum("ml,l...->m...", matrix, field, precision=lax.Precision.HIGH)


def laplace(padded):
    center = padded[:, 1:-1, 1:-1]
    beside_all = (
        padded[:, 2:, 1:-1] + padded[:, :-2, 1:-1] + padded[:, 1:-1, 2:] + padded[:, 1:-1, :-2]
    )
    return beside_all - 4.0 * center


def inner_step(padded, coeff, vert_mix):
    center = padded[:, 1:-1, 1:-1]
    beside_all = (
        padded[:, 2:, 1:-1] + padded[:, :-2, 1:-1] + padded[:, 1:-1, 2:] + padded[:, 1:-1, :-2]
    )
    return center + coeff[None] * (beside_all - 4.0 * center) + level_mix(vert_mix, center)


def block_product(weights, picked):
    return jnp.einsum("okij,fokj->foi", weights, picked, preferred_element_type=jnp.float32)


def near_index(cols, per_tile, tiles, here):
    relative = (cols // per_tile - here + 2) % tiles
    return relative * per_tile + cols % per_tile


def pick(local, base, piece, count):
    ids = base + jnp.arange(count, dtype=local.dtype)
    onehot = (local[:, None] == ids[None, :]).astype(piece.dtype)
    return jnp.einsum("qb,fbj->fqj", onehot, piece, preferred_element_type=jnp.float32)


def exchange_and_pick(blocks, cols, here):
    fields, per_tile, cells = blocks.shape
    tiles = lax.axis_size("tile")
    local = near_index(cols, per_tile, tiles, here).reshape(-1)
    even = here % 2 == 0
    chip_even = (here // 2) % 2 == 0
    first = swap(blocks, "tile", 2, 0)
    second = swap(blocks, "tile", 2, 1)
    first_base = jnp.where(chip_even, 4 * per_tile, 0)
    second_base = 4 * per_tile - first_base
    forward = jnp.where(even == chip_even, first, second)
    bundle = jnp.concatenate([blocks, forward], axis=1)
    partner = swap(bundle, "tile", 1, 0)
    plus_one = jnp.where(even, 0, per_tile)
    minus_one = per_tile - plus_one
    slot = local // per_tile
    within = local % per_tile
    partner_local = jnp.where(slot == 3, plus_one + within, jnp.where(slot == 1, minus_one + within, -1))
    picked = pick(local, 2 * per_tile, blocks, per_tile)
    picked = picked + pick(local, first_base, first, per_tile)
    picked = picked + pick(local, second_base, second, per_tile)
    picked = picked + pick(partner_local, 0, partner, 2 * per_tile)
    return picked.astype(blocks.dtype).reshape((fields,) + cols.shape + (cells,)), first


def body(
    atm_state,
    kappa,
    vert_mix,
    flux_proj,
    remap_weight,
    remap_cols,
    ocean_state,
    ocean_mix,
    forcing,
    wet_mask,
    surface_proj,
    back_weight,
    back_cols,
    back_proj,
):
    levels, rows_here, cols_here = atm_state.shape
    joined = jnp.concatenate([atm_state, kappa[None]], axis=0)
    padded = halo_rows(halo_cols(joined, 2), 2)
    field = padded[:levels]
    coeff = padded[levels]
    inner = coeff[1:-1, 1:-1]
    centre = coeff[2:-2, 2:-2]
    step = jnp.eye(levels, dtype=vert_mix.dtype) + vert_mix
    once = jnp.dot(flux_proj, step, precision=lax.Precision.HIGHEST)
    twice = jnp.dot(once, step, precision=lax.Precision.HIGHEST)
    fields = flux_proj.shape[0]
    stacked = level_mix(jnp.concatenate([flux_proj, once, twice], axis=0), field)
    plain, mixed_once, mixed_twice = stacked[:fields], stacked[fields:2 * fields], stacked[2 * fields:]
    proj_first = mixed_once[:, 1:-1, 1:-1] + inner[None] * laplace(plain)
    proj_mixed = mixed_twice[:, 2:-2, 2:-2] + centre[None] * laplace(mixed_once)[:, 1:-1, 1:-1]
    surface = (proj_mixed + centre[None] * laplace(proj_first)).astype(jnp.bfloat16)
    atm_blocks = rows_here * cols_here // 64
    surface_blocks = surface.reshape(fields, atm_blocks, 64)
    ocean_blocks = remap_weight.shape[0]
    here = lax.axis_index("tile")
    mixed = lax.optimization_barrier(
        ocean_state + jnp.dot(ocean_mix, ocean_state, precision=lax.Precision.HIGHEST)
    )
    remapped = block_product(remap_weight, exchange_and_pick(surface_blocks, remap_cols, here)[0])
    field = lax.optimization_barrier((field, remapped))[0]
    atm_mid = inner_step(inner_step(field, inner, vert_mix), centre, vert_mix)
    remapped = remapped.reshape(fields, ocean_blocks * 64)
    wet = wet_mask[None] == 1
    stepped = mixed + jnp.dot(forcing, remapped, precision=lax.Precision.HIGH)
    ocean_out = jnp.where(wet, stepped, ocean_state)
    settled = jnp.dot(surface_proj, jnp.where(wet, mixed, ocean_state), precision=lax.Precision.HIGHEST)
    sea_forcing = jnp.dot(surface_proj, forcing, precision=lax.Precision.HIGHEST)
    moved = jnp.dot(sea_forcing, remapped, precision=lax.Precision.HIGH)
    sea = (settled + jnp.where(wet, moved, 0.0)).astype(jnp.bfloat16)
    sea_blocks = sea.reshape(sea.shape[0], ocean_blocks, 64)
    returned = block_product(back_weight, exchange_and_pick(sea_blocks, back_cols, here)[0])
    returned = returned.reshape(sea.shape[0], rows_here, cols_here)
    atm_out = atm_mid + level_mix(back_proj, returned)
    return (atm_out, ocean_out)


def solution(mesh):
    return jax.shard_map(
        body,
        mesh=mesh,
        in_specs=(
            P(None, "comp", "tile"),
            P("comp", "tile"),
            P(),
            P(),
            P(("comp", "tile"), None, None, None),
            P(("comp", "tile"), None),
            P(None, ("comp", "tile")),
            P(),
            P(),
            P(("comp", "tile")),
            P(),
            P(("comp", "tile"), None, None, None),
            P(("comp", "tile"), None),
            P(),
        ),
        out_specs=(P(None, "comp", "tile"), P(None, ("comp", "tile"))),
        check_vma=False,
    )
```

```python
import jax
import jax.numpy as jnp
from jax import lax
from jax.sharding import PartitionSpec as P


def from_behind(value, axis, steps):
    count = lax.axis_size(axis)
    pairs = [(source, (source + steps) % count) for source in range(count)]
    return lax.ppermute(value, axis, pairs)


def swap(value, axis, stride, phase):
    count = lax.axis_size(axis)
    groups = count // stride
    pairs = []
    for source in range(count):
        group = source // stride
        step = 1 if group % 2 == phase else -1
        pairs.append((source, ((group + step) % groups) * stride + source % stride))
    return lax.ppermute(value, axis, pairs)


def halo_cols(cells, width):
    levels, rows, cols = cells.shape
    even = lax.axis_index("tile") % 2 == 0
    head = cells[:, :, :width].reshape(-1)
    tail = cells[:, :, cols - width:].reshape(-1)
    partner = swap(jnp.where(even, tail, head), "tile", 1, 0)
    cross = swap(jnp.where(even, head, tail), "tile", 1, 1)
    left = jnp.where(even, cross, partner).reshape(levels, rows, width)
    right = jnp.where(even, partner, cross).reshape(levels, rows, width)
    return jnp.concatenate([left, cells, right], axis=2)


def halo_rows(cells, width):
    levels, rows, cols = cells.shape
    even = lax.axis_index("comp") % 2 == 0
    head = cells[:, :width, :]
    tail = cells[:, rows - width:, :]
    first = swap(jnp.where(even, tail, head), "comp", 1, 0)
    second = swap(jnp.where(even, head, tail), "comp", 1, 1)
    up = jnp.where(even, second, first)
    down = jnp.where(even, first, second)
    return jnp.concatenate([up, cells, down], axis=1)


def level_mix(matrix, field):
    return jnp.einsum("ml,l...->m...", matrix, field, precision=lax.Precision.HIGHEST)


def inner_step(padded, coeff, vert_mix):
    center = padded[:, 1:-1, 1:-1]
    beside_all = (
        padded[:, 2:, 1:-1] + padded[:, :-2, 1:-1] + padded[:, 1:-1, 2:] + padded[:, 1:-1, :-2]
    )
    return center + coeff[None] * (beside_all - 4.0 * center) + level_mix(vert_mix, center)


def block_product(weights, picked):
    return jnp.einsum("okij,fokj->foi", weights, picked, preferred_element_type=jnp.float32)


def near_index(cols, per_tile, tiles, here):
    relative = (cols // per_tile - here + 2) % tiles
    return relative * per_tile + cols % per_tile


def pick(local, base, piece, count):
    ids = base + jnp.arange(count, dtype=local.dtype)
    onehot = (local[:, None] == ids[None, :]).astype(piece.dtype)
    return jnp.einsum("qb,fbj->fqj", onehot, piece, preferred_element_type=jnp.float32)


def exchange_and_pick(blocks, cols, here):
    fields, per_tile, cells = blocks.shape
    tiles = lax.axis_size("tile")
    local = near_index(cols, per_tile, tiles, here).reshape(-1)
    even = here % 2 == 0
    chip_even = (here // 2) % 2 == 0
    first = swap(blocks, "tile", 2, 0)
    second = swap(blocks, "tile", 2, 1)
    first_base = jnp.where(chip_even, 4 * per_tile, 0)
    second_base = 4 * per_tile - first_base
    forward = jnp.where(even == chip_even, first, second)
    bundle = jnp.concatenate([blocks, forward], axis=1)
    partner = swap(bundle, "tile", 1, 0)
    plus_one = jnp.where(even, 0, per_tile)
    minus_one = per_tile - plus_one
    slot = local // per_tile
    within = local % per_tile
    partner_local = jnp.where(slot == 3, plus_one + within, jnp.where(slot == 1, minus_one + within, -1))
    picked = pick(local, 2 * per_tile, blocks, per_tile)
    picked = picked + pick(local, first_base, first, per_tile)
    picked = picked + pick(local, second_base, second, per_tile)
    picked = picked + pick(partner_local, 0, partner, 2 * per_tile)
    return picked.astype(blocks.dtype).reshape((fields,) + cols.shape + (cells,))


def body(
    atm_state,
    kappa,
    vert_mix,
    flux_proj,
    remap_weight,
    remap_cols,
    ocean_state,
    ocean_mix,
    forcing,
    wet_mask,
    surface_proj,
    back_weight,
    back_cols,
    back_proj,
):
    levels, rows_here, cols_here = atm_state.shape
    joined = jnp.concatenate([atm_state, kappa[None]], axis=0)
    padded = halo_rows(halo_cols(joined, 2), 2)
    field = padded[:levels]
    coeff = padded[levels]
    first = inner_step(field, coeff[1:-1, 1:-1], vert_mix)
    atm_mid = inner_step(first, coeff[2:-2, 2:-2], vert_mix)
    surface = level_mix(flux_proj, atm_mid).astype(jnp.bfloat16)
    fields = surface.shape[0]
    atm_blocks = rows_here * cols_here // 64
    surface_blocks = surface.reshape(fields, atm_blocks, 64)
    ocean_blocks = remap_weight.shape[0]
    here = lax.axis_index("tile")
    mixed = lax.optimization_barrier(
        ocean_state + jnp.dot(ocean_mix, ocean_state, precision=lax.Precision.HIGHEST)
    )
    remapped = block_product(remap_weight, exchange_and_pick(surface_blocks, remap_cols, here))
    remapped = remapped.reshape(fields, ocean_blocks * 64)
    wet = wet_mask[None] == 1
    stepped = mixed + jnp.dot(forcing, remapped, precision=lax.Precision.HIGHEST)
    ocean_out = jnp.where(wet, stepped, ocean_state)
    settled = jnp.dot(surface_proj, jnp.where(wet, mixed, ocean_state), precision=lax.Precision.HIGHEST)
    sea_forcing = jnp.dot(surface_proj, forcing, precision=lax.Precision.HIGHEST)
    moved = jnp.dot(sea_forcing, remapped, precision=lax.Precision.HIGHEST)
    sea = (settled + jnp.where(wet, moved, 0.0)).astype(jnp.bfloat16)
    sea_blocks = sea.reshape(sea.shape[0], ocean_blocks, 64)
    returned = block_product(back_weight, exchange_and_pick(sea_blocks, back_cols, here))
    returned = returned.reshape(sea.shape[0], rows_here, cols_here)
    atm_out = atm_mid + level_mix(back_proj, returned)
    return (atm_out, ocean_out)


def solution(mesh):
    return jax.shard_map(
        body,
        mesh=mesh,
        in_specs=(
            P(None, "comp", "tile"),
            P("comp", "tile"),
            P(),
            P(),
            P(("comp", "tile"), None, None, None),
            P(("comp", "tile"), None),
            P(None, ("comp", "tile")),
            P(),
            P(),
            P(("comp", "tile")),
            P(),
            P(("comp", "tile"), None, None, None),
            P(("comp", "tile"), None),
            P(),
        ),
        out_specs=(P(None, "comp", "tile"), P(None, ("comp", "tile"))),
        check_vma=False,
    )
```

```python
import jax
import jax.numpy as jnp
from jax import lax
from jax.sharding import PartitionSpec as P


def from_behind(value, axis, steps):
    count = lax.axis_size(axis)
    pairs = [(source, (source + steps) % count) for source in range(count)]
    return lax.ppermute(value, axis, pairs)


def swap(value, axis, stride, phase):
    count = lax.axis_size(axis)
    groups = count // stride
    pairs = []
    for source in range(count):
        group = source // stride
        step = 1 if group % 2 == phase else -1
        pairs.append((source, ((group + step) % groups) * stride + source % stride))
    return lax.ppermute(value, axis, pairs)


def halo_cols(cells, width):
    levels, rows, cols = cells.shape
    even = lax.axis_index("tile") % 2 == 0
    head = cells[:, :, :width].reshape(-1)
    tail = cells[:, :, cols - width:].reshape(-1)
    partner = swap(jnp.where(even, tail, head), "tile", 1, 0)
    cross = swap(jnp.where(even, head, tail), "tile", 1, 1)
    left = jnp.where(even, cross, partner).reshape(levels, rows, width)
    right = jnp.where(even, partner, cross).reshape(levels, rows, width)
    return jnp.concatenate([left, cells, right], axis=2)


def halo_rows(cells, width):
    levels, rows, cols = cells.shape
    even = lax.axis_index("comp") % 2 == 0
    head = cells[:, :width, :]
    tail = cells[:, rows - width:, :]
    first = swap(jnp.where(even, tail, head), "comp", 1, 0)
    second = swap(jnp.where(even, head, tail), "comp", 1, 1)
    up = jnp.where(even, second, first)
    down = jnp.where(even, first, second)
    return jnp.concatenate([up, cells, down], axis=1)


def level_mix(matrix, field):
    return jnp.einsum("ml,l...->m...", matrix, field, precision=lax.Precision.HIGH)


def inner_step(padded, coeff, vert_mix):
    center = padded[:, 1:-1, 1:-1]
    beside_all = (
        padded[:, 2:, 1:-1] + padded[:, :-2, 1:-1] + padded[:, 1:-1, 2:] + padded[:, 1:-1, :-2]
    )
    return center + coeff[None] * (beside_all - 4.0 * center) + level_mix(vert_mix, center)


def block_product(weights, picked):
    return jnp.einsum("okij,fokj->foi", weights, picked, preferred_element_type=jnp.float32)


def near_index(cols, per_tile, tiles, here):
    relative = (cols // per_tile - here + 2) % tiles
    return relative * per_tile + cols % per_tile


def pick(local, base, piece, count):
    ids = base + jnp.arange(count, dtype=local.dtype)
    onehot = (local[:, None] == ids[None, :]).astype(piece.dtype)
    return jnp.einsum("qb,fbj->fqj", onehot, piece, preferred_element_type=jnp.float32)


def exchange_and_pick(blocks, cols, here):
    fields, per_tile, cells = blocks.shape
    tiles = lax.axis_size("tile")
    local = near_index(cols, per_tile, tiles, here).reshape(-1)
    even = here % 2 == 0
    chip_even = (here // 2) % 2 == 0
    first = swap(blocks, "tile", 2, 0)
    second = swap(blocks, "tile", 2, 1)
    first_base = jnp.where(chip_even, 4 * per_tile, 0)
    second_base = 4 * per_tile - first_base
    forward = jnp.where(even == chip_even, first, second)
    bundle = jnp.concatenate([blocks, forward], axis=1)
    partner = swap(bundle, "tile", 1, 0)
    plus_one = jnp.where(even, 0, per_tile)
    minus_one = per_tile - plus_one
    slot = local // per_tile
    within = local % per_tile
    partner_local = jnp.where(slot == 3, plus_one + within, jnp.where(slot == 1, minus_one + within, -1))
    picked = pick(local, 2 * per_tile, blocks, per_tile)
    picked = picked + pick(local, first_base, first, per_tile)
    picked = picked + pick(local, second_base, second, per_tile)
    picked = picked + pick(partner_local, 0, partner, 2 * per_tile)
    return picked.astype(blocks.dtype).reshape((fields,) + cols.shape + (cells,))


def body(
    atm_state,
    kappa,
    vert_mix,
    flux_proj,
    remap_weight,
    remap_cols,
    ocean_state,
    ocean_mix,
    forcing,
    wet_mask,
    surface_proj,
    back_weight,
    back_cols,
    back_proj,
):
    levels, rows_here, cols_here = atm_state.shape
    joined = jnp.concatenate([atm_state, kappa[None]], axis=0)
    padded = halo_rows(halo_cols(joined, 2), 2)
    field = padded[:levels]
    coeff = padded[levels]
    first = inner_step(field, coeff[1:-1, 1:-1], vert_mix)
    atm_mid = inner_step(first, coeff[2:-2, 2:-2], vert_mix)
    surface = level_mix(flux_proj, atm_mid).astype(jnp.bfloat16)
    fields = surface.shape[0]
    atm_blocks = rows_here * cols_here // 64
    surface_blocks = surface.reshape(fields, atm_blocks, 64)
    ocean_blocks = remap_weight.shape[0]
    here = lax.axis_index("tile")
    mixed = lax.optimization_barrier(
        ocean_state + jnp.dot(ocean_mix, ocean_state, precision=lax.Precision.HIGHEST)
    )
    remapped = block_product(remap_weight, exchange_and_pick(surface_blocks, remap_cols, here))
    remapped = remapped.reshape(fields, ocean_blocks * 64)
    stepped = mixed + jnp.dot(forcing, remapped, precision=lax.Precision.HIGH)
    ocean_out = jnp.where(wet_mask[None] == 1, stepped, ocean_state)
    sea = jnp.dot(surface_proj, ocean_out, precision=lax.Precision.HIGH).astype(jnp.bfloat16)
    sea_blocks = sea.reshape(sea.shape[0], ocean_blocks, 64)
    returned = block_product(back_weight, exchange_and_pick(sea_blocks, back_cols, here))
    returned = returned.reshape(sea.shape[0], rows_here, cols_here)
    atm_out = atm_mid + level_mix(back_proj, returned)
    return (atm_out, ocean_out)


def solution(mesh):
    return jax.shard_map(
        body,
        mesh=mesh,
        in_specs=(
            P(None, "comp", "tile"),
            P("comp", "tile"),
            P(),
            P(),
            P(("comp", "tile"), None, None, None),
            P(("comp", "tile"), None),
            P(None, ("comp", "tile")),
            P(),
            P(),
            P(("comp", "tile")),
            P(),
            P(("comp", "tile"), None, None, None),
            P(("comp", "tile"), None),
            P(),
        ),
        out_specs=(P(None, "comp", "tile"), P(None, ("comp", "tile"))),
        check_vma=False,
    )
```

```python
import jax
import jax.numpy as jnp
from jax import lax
from jax.sharding import PartitionSpec as P


def from_behind(value, axis, steps):
    count = lax.axis_size(axis)
    pairs = [(source, (source + steps) % count) for source in range(count)]
    return lax.ppermute(value, axis, pairs)


def swap(value, axis, stride, phase):
    count = lax.axis_size(axis)
    groups = count // stride
    pairs = []
    for source in range(count):
        group = source // stride
        step = 1 if group % 2 == phase else -1
        pairs.append((source, ((group + step) % groups) * stride + source % stride))
    return lax.ppermute(value, axis, pairs)


def halo_cols(cells, width):
    levels, rows, cols = cells.shape
    even = lax.axis_index("tile") % 2 == 0
    head = cells[:, :, :width].reshape(-1)
    tail = cells[:, :, cols - width:].reshape(-1)
    partner = swap(jnp.where(even, tail, head), "tile", 1, 0)
    cross = swap(jnp.where(even, head, tail), "tile", 1, 1)
    left = jnp.where(even, cross, partner).reshape(levels, rows, width)
    right = jnp.where(even, partner, cross).reshape(levels, rows, width)
    return jnp.concatenate([left, cells, right], axis=2)


def halo_rows(cells, width):
    levels, rows, cols = cells.shape
    even = lax.axis_index("comp") % 2 == 0
    head = cells[:, :width, :]
    tail = cells[:, rows - width:, :]
    first = swap(jnp.where(even, tail, head), "comp", 1, 0)
    second = swap(jnp.where(even, head, tail), "comp", 1, 1)
    up = jnp.where(even, second, first)
    down = jnp.where(even, first, second)
    return jnp.concatenate([up, cells, down], axis=1)


def level_mix(matrix, field):
    return jnp.einsum("ml,l...->m...", matrix, field, precision=lax.Precision.HIGH)


def inner_step(padded, coeff, vert_mix):
    center = padded[:, 1:-1, 1:-1]
    beside_all = (
        padded[:, 2:, 1:-1] + padded[:, :-2, 1:-1] + padded[:, 1:-1, 2:] + padded[:, 1:-1, :-2]
    )
    return center + coeff[None] * (beside_all - 4.0 * center) + level_mix(vert_mix, center)


def block_product(weights, picked):
    return jnp.einsum("okij,fokj->foi", weights, picked, preferred_element_type=jnp.float32)


def near_index(cols, per_tile, tiles, here):
    relative = (cols // per_tile - here + 2) % tiles
    return relative * per_tile + cols % per_tile


def pick(local, base, piece, count):
    ids = base + jnp.arange(count, dtype=local.dtype)
    onehot = (local[:, None] == ids[None, :]).astype(piece.dtype)
    return jnp.einsum("qb,fbj->fqj", onehot, piece, preferred_element_type=jnp.float32)


def exchange_and_pick(blocks, cols, here):
    fields, per_tile, cells = blocks.shape
    tiles = lax.axis_size("tile")
    local = near_index(cols, per_tile, tiles, here).reshape(-1)
    even = here % 2 == 0
    forward = lax.ppermute(blocks, "tile", [(s, (s - 2 if s % 2 == 0 else s + 2) % tiles) for s in range(tiles)])
    other = lax.ppermute(blocks, "tile", [(s, (s + 2 if s % 2 == 0 else s - 2) % tiles) for s in range(tiles)])
    first_base = jnp.where(even, 4 * per_tile, 0)
    second_base = 4 * per_tile - first_base
    bundle = jnp.concatenate([blocks, forward], axis=1)
    partner = swap(bundle, "tile", 1, 0)
    plus_one = jnp.where(even, 0, per_tile)
    minus_one = per_tile - plus_one
    slot = local // per_tile
    within = local % per_tile
    partner_local = jnp.where(slot == 3, plus_one + within, jnp.where(slot == 1, minus_one + within, -1))
    picked = pick(local, 2 * per_tile, blocks, per_tile)
    picked = picked + pick(local, first_base, forward, per_tile)
    picked = picked + pick(local, second_base, other, per_tile)
    picked = picked + pick(partner_local, 0, partner, 2 * per_tile)
    return picked.astype(blocks.dtype).reshape((fields,) + cols.shape + (cells,))


def body(
    atm_state,
    kappa,
    vert_mix,
    flux_proj,
    remap_weight,
    remap_cols,
    ocean_state,
    ocean_mix,
    forcing,
    wet_mask,
    surface_proj,
    back_weight,
    back_cols,
    back_proj,
):
    levels, rows_here, cols_here = atm_state.shape
    joined = jnp.concatenate([atm_state, kappa[None]], axis=0)
    padded = halo_rows(halo_cols(joined, 2), 2)
    field = padded[:levels]
    coeff = padded[levels]
    first = inner_step(field, coeff[1:-1, 1:-1], vert_mix)
    atm_mid = inner_step(first, coeff[2:-2, 2:-2], vert_mix)
    surface = level_mix(flux_proj, atm_mid).astype(jnp.bfloat16)
    fields = surface.shape[0]
    atm_blocks = rows_here * cols_here // 64
    surface_blocks = surface.reshape(fields, atm_blocks, 64)
    ocean_blocks = remap_weight.shape[0]
    here = lax.axis_index("tile")
    mixed = lax.optimization_barrier(
        ocean_state + jnp.dot(ocean_mix, ocean_state, precision=lax.Precision.HIGHEST)
    )
    remapped = block_product(remap_weight, exchange_and_pick(surface_blocks, remap_cols, here))
    remapped = remapped.reshape(fields, ocean_blocks * 64)
    stepped = mixed + jnp.dot(forcing, remapped, precision=lax.Precision.HIGH)
    ocean_out = jnp.where(wet_mask[None] == 1, stepped, ocean_state)
    sea = jnp.dot(surface_proj, ocean_out, precision=lax.Precision.HIGH).astype(jnp.bfloat16)
    sea_blocks = sea.reshape(sea.shape[0], ocean_blocks, 64)
    returned = block_product(back_weight, exchange_and_pick(sea_blocks, back_cols, here))
    returned = returned.reshape(sea.shape[0], rows_here, cols_here)
    atm_out = atm_mid + level_mix(back_proj, returned)
    return (atm_out, ocean_out)


def solution(mesh):
    return jax.shard_map(
        body,
        mesh=mesh,
        in_specs=(
            P(None, "comp", "tile"),
            P("comp", "tile"),
            P(),
            P(),
            P(("comp", "tile"), None, None, None),
            P(("comp", "tile"), None),
            P(None, ("comp", "tile")),
            P(),
            P(),
            P(("comp", "tile")),
            P(),
            P(("comp", "tile"), None, None, None),
            P(("comp", "tile"), None),
            P(),
        ),
        out_specs=(P(None, "comp", "tile"), P(None, ("comp", "tile"))),
        check_vma=False,
    )
```

```python
import jax
import jax.numpy as jnp
from jax import lax
from jax.sharding import PartitionSpec as P


def from_behind(value, axis, steps):
    count = lax.axis_size(axis)
    pairs = [(source, (source + steps) % count) for source in range(count)]
    return lax.ppermute(value, axis, pairs)


def swap(value, axis, stride, phase):
    count = lax.axis_size(axis)
    groups = count // stride
    pairs = []
    for source in range(count):
        group = source // stride
        step = 1 if group % 2 == phase else -1
        pairs.append((source, ((group + step) % groups) * stride + source % stride))
    return lax.ppermute(value, axis, pairs)


def halo_cols(cells, width):
    levels, rows, cols = cells.shape
    even = lax.axis_index("tile") % 2 == 0
    head = cells[:, :, :width].reshape(-1)
    tail = cells[:, :, cols - width:].reshape(-1)
    partner = swap(jnp.where(even, tail, head), "tile", 1, 0)
    cross = swap(jnp.where(even, head, tail), "tile", 1, 1)
    left = jnp.where(even, cross, partner).reshape(levels, rows, width)
    right = jnp.where(even, partner, cross).reshape(levels, rows, width)
    return jnp.concatenate([left, cells, right], axis=2)


def halo_rows(cells, width):
    levels, rows, cols = cells.shape
    even = lax.axis_index("comp") % 2 == 0
    head = cells[:, :width, :]
    tail = cells[:, rows - width:, :]
    first = swap(jnp.where(even, tail, head), "comp", 1, 0)
    second = swap(jnp.where(even, head, tail), "comp", 1, 1)
    up = jnp.where(even, second, first)
    down = jnp.where(even, first, second)
    return jnp.concatenate([up, cells, down], axis=1)


def level_mix(matrix, field):
    return jnp.einsum("ml,l...->m...", matrix, field, precision=lax.Precision.HIGH)


def inner_step(padded, coeff, vert_mix):
    center = padded[:, 1:-1, 1:-1]
    beside_all = (
        padded[:, 2:, 1:-1] + padded[:, :-2, 1:-1] + padded[:, 1:-1, 2:] + padded[:, 1:-1, :-2]
    )
    return center + coeff[None] * (beside_all - 4.0 * center) + level_mix(vert_mix, center)


def block_product(weights, picked):
    return jnp.einsum("okij,fokj->foi", weights, picked, preferred_element_type=jnp.float32)


def near_index(cols, per_tile, tiles, here):
    relative = (cols // per_tile - here + 2) % tiles
    return relative * per_tile + cols % per_tile


def pick(local, base, piece, count):
    ids = base + jnp.arange(count, dtype=local.dtype)
    onehot = (local[:, None] == ids[None, :]).astype(piece.dtype)
    return jnp.einsum("qb,fbj->fqj", onehot, piece, preferred_element_type=jnp.float32)


def exchange_and_pick(blocks, cols, here):
    fields, per_tile, cells = blocks.shape
    tiles = lax.axis_size("tile")
    local = near_index(cols, per_tile, tiles, here).reshape(-1)
    even = here % 2 == 0
    forward = lax.ppermute(blocks, "tile", [(s, (s - 2 if s % 2 == 0 else s + 2) % tiles) for s in range(tiles)])
    other = lax.ppermute(blocks, "tile", [(s, (s + 2 if s % 2 == 0 else s - 2) % tiles) for s in range(tiles)])
    first_base = jnp.where(even, 4 * per_tile, 0)
    second_base = 4 * per_tile - first_base
    bundle = jnp.concatenate([blocks, forward], axis=1)
    partner = swap(bundle, "tile", 1, 0)
    plus_one = jnp.where(even, 0, per_tile)
    minus_one = per_tile - plus_one
    slot = local // per_tile
    within = local % per_tile
    partner_local = jnp.where(slot == 3, plus_one + within, jnp.where(slot == 1, minus_one + within, -1))
    early = pick(local, 2 * per_tile, blocks, per_tile)
    early = early + pick(local, first_base, forward, per_tile)
    early = early + pick(partner_local, 0, partner, 2 * per_tile)
    shape = (fields,) + cols.shape + (cells,)
    def finish(early_product):
        later, early_product = lax.optimization_barrier((other, early_product))
        late = pick(local, second_base, later, per_tile).astype(blocks.dtype).reshape(shape)
        return early_product, late

    return early.astype(blocks.dtype).reshape(shape), finish


def body(
    atm_state,
    kappa,
    vert_mix,
    flux_proj,
    remap_weight,
    remap_cols,
    ocean_state,
    ocean_mix,
    forcing,
    wet_mask,
    surface_proj,
    back_weight,
    back_cols,
    back_proj,
):
    levels, rows_here, cols_here = atm_state.shape
    joined = jnp.concatenate([atm_state, kappa[None]], axis=0)
    padded = halo_rows(halo_cols(joined, 2), 2)
    field = padded[:levels]
    coeff = padded[levels]
    first = inner_step(field, coeff[1:-1, 1:-1], vert_mix)
    atm_mid = inner_step(first, coeff[2:-2, 2:-2], vert_mix)
    surface = level_mix(flux_proj, atm_mid).astype(jnp.bfloat16)
    fields = surface.shape[0]
    atm_blocks = rows_here * cols_here // 64
    surface_blocks = surface.reshape(fields, atm_blocks, 64)
    ocean_blocks = remap_weight.shape[0]
    here = lax.axis_index("tile")
    mixed = lax.optimization_barrier(
        ocean_state + jnp.dot(ocean_mix, ocean_state, precision=lax.Precision.HIGHEST)
    )
    early, finish = exchange_and_pick(surface_blocks, remap_cols, here)
    first_part, late = finish(block_product(remap_weight, early))
    remapped = first_part + block_product(remap_weight, late)
    remapped = remapped.reshape(fields, ocean_blocks * 64)
    stepped = mixed + jnp.dot(forcing, remapped, precision=lax.Precision.HIGH)
    ocean_out = jnp.where(wet_mask[None] == 1, stepped, ocean_state)
    sea = jnp.dot(surface_proj, ocean_out, precision=lax.Precision.HIGH).astype(jnp.bfloat16)
    sea_blocks = sea.reshape(sea.shape[0], ocean_blocks, 64)
    early, finish = exchange_and_pick(sea_blocks, back_cols, here)
    first_part, late = finish(block_product(back_weight, early))
    returned = first_part + block_product(back_weight, late)
    returned = returned.reshape(sea.shape[0], rows_here, cols_here)
    atm_out = atm_mid + level_mix(back_proj, returned)
    return (atm_out, ocean_out)


def solution(mesh):
    return jax.shard_map(
        body,
        mesh=mesh,
        in_specs=(
            P(None, "comp", "tile"),
            P("comp", "tile"),
            P(),
            P(),
            P(("comp", "tile"), None, None, None),
            P(("comp", "tile"), None),
            P(None, ("comp", "tile")),
            P(),
            P(),
            P(("comp", "tile")),
            P(),
            P(("comp", "tile"), None, None, None),
            P(("comp", "tile"), None),
            P(),
        ),
        out_specs=(P(None, "comp", "tile"), P(None, ("comp", "tile"))),
        check_vma=False,
    )
```
